512 devices in a mesh: dir: 4 (over y_hi, core), chan: 128 (over z, y_lo, x).
Axes of the slice: x: 4, y: 8 (y_hi: 2, y_lo: 4; y = y_hi * 4 + y_lo), z: 8, core: 2. Of those that a mesh axis runs over, the one named last changes fastest.
Arguments:
- visibilities: float32 [256, 1, 2, 2, 2850], P('chan'), may hold values from -6 to 6
- model: bfloat16 [32, 256, 1, 2, 2, 2850], P('dir', 'chan'), may hold values from -4 to 4
- gains: float32 [32, 256, 2, 2, 76], P('dir', 'chan'), may hold values from -1 to 1
- weights: float32 [256], P('chan'), may hold values from 0.2 to 5
- widths: int32 [256], P('chan'), may hold values from 1 to 2
- baseline_table: int32 [2, 2850], replicated, may hold values from 0 to 75, as said below
Outputs:
- new_gains: float32 [32, 256, 2, 2, 76], P('dir', 'chan')
- residual: float32 [256, 1, 2, 2, 2850], P('chan')
The draws below stay inside these ranges and needn't reach their ends.
Inputs may be any that keep to these rules, and one draw needn't show every extreme that they name: `baseline_table`: each column names two different stations; every unordered pair of stations appears in exactly one column.
All inputs are finite; a program needn't handle non-finite values.
Results may differ from the reference program's by a relative error of at most 0.00035.
Values sent between devices are 32-bit elements; how exact they have to be, the bound alone decides.
No kernel may reach another device: no remote copies, remote signals or barrier semaphores. Data moves between devices by JAX's collectives and lax.ppermute only.
A program may use at most 64 MiB of HBM per device.

```python
import math
import jax
import jax.numpy as jnp
import numpy as np
from jax import lax

STATIONS = 76
BASELINE_COUNT = 2850
DIRECTION_COUNT = 32
CHANNEL_COUNT = 256
TIME_SAMPLES = 1
SPAN = 2
ITERS = 2


def draw_widths(key, part):
    base = jax.random.randint(jax.random.fold_in(key, 11), (CHANNEL_COUNT,), 1, SPAN + 1)
    spots = jax.random.randint(jax.random.fold_in(key, 12), (2,), 0, CHANNEL_COUNT)
    base = base.at[spots[0]].set(1)
    base = base.at[spots[1]].set(SPAN)
    return base.astype(jnp.int32)


def draw_baseline_table(key, part):
    first, second = np.triu_indices(STATIONS, 1)
    first = jnp.asarray(first.astype(np.int32))
    second = jnp.asarray(second.astype(np.int32))
    station_ordering = jax.random.permutation(jax.random.fold_in(key, 21), BASELINE_COUNT)
    first = first[station_ordering]
    second = second[station_ordering]
    reversed_pairs = jax.random.randint(jax.random.fold_in(key, 22), (BASELINE_COUNT,), 0, 2)
    left = jnp.where(reversed_pairs == 1, second, first)
    right = jnp.where(reversed_pairs == 1, first, second)
    return jnp.stack([left, right]).astype(jnp.int32)


def shard_levels(key, shape, pieces, least, top_value):
    def one(dim, shards_of):
        draws = jax.random.uniform(jax.random.fold_in(jax.random.fold_in(key, 6), dim), (shards_of,), jnp.float32, least / len(pieces), top_value / len(pieces))
        return jnp.repeat(jnp.exp(draws), shape[dim] // shards_of).reshape((-1,) + (1,) * (len(shape) - dim - 1))

    gain = one(*pieces[0])
    for cut in pieces[1:]:
        gain = gain * one(*cut)
    return gain


def gaussian(own_key, extent, scale, most, pieces=(), kind=jnp.bfloat16):
    drawn = jax.random.normal(own_key, extent, jnp.float32) * scale
    if len(pieces) > 0:
        drawn = shard_levels(own_key, extent, pieces, -0.22, 0.18) * drawn
    return jnp.clip(drawn, min=-most, max=most).astype(kind)


def setup_inputs(seed: int = 0) -> dict:
    key_list = jax.random.split(jax.random.key(seed), 7)
    visibilities = gaussian(key_list[0], (CHANNEL_COUNT, TIME_SAMPLES, 2, 2, BASELINE_COUNT), 1.0, 6.0, ((0, 128),), jnp.float32)
    model = gaussian(key_list[1], (DIRECTION_COUNT, CHANNEL_COUNT, TIME_SAMPLES, 2, 2, BASELINE_COUNT), 0.3, 4.0, ((0, 4), (1, 128)))
    gains = jnp.clip(jax.random.uniform(key_list[2], (DIRECTION_COUNT, CHANNEL_COUNT, 2, 2, STATIONS), jnp.float32, -1.0, 1.0) * shard_levels(key_list[2], (DIRECTION_COUNT, CHANNEL_COUNT, 2, 2, STATIONS), ((0, 4), (1, 128)), -0.4, 0.0), -1.0, 1.0)
    weights = jnp.clip(jnp.exp(math.log(5.0) - 3.218876 * jax.random.uniform(key_list[3], (CHANNEL_COUNT,), jnp.float32) ** shard_levels(key_list[3], (CHANNEL_COUNT,), ((0, 128),), -0.2, 0.2)), 0.2, 5.0)
    widths = draw_widths(jax.random.fold_in(key_list[6], 71), 0)
    baseline_table = draw_baseline_table(jax.random.fold_in(key_list[6], 71), 0)
    return dict(visibilities=visibilities, model=model, gains=gains, weights=weights, widths=widths, baseline_table=baseline_table)


step_size = 0.6
epsilon = 1e-6
highest = lax.Precision.HIGHEST


def station_tables(baseline_table):
    column = jnp.arange(STATIONS, dtype=jnp.int32)[:, None]
    left_hot = (baseline_table[0][None, :] == column).astype(jnp.float32)
    right_hot = (baseline_table[1][None, :] == column).astype(jnp.float32)
    return left_hot, right_hot


def corrupt(gains, model, left_hot, right_hot):
    model = model.astype(jnp.float32)
    left_gain = jnp.matmul(gains, left_hot, precision=highest)[:, None]
    right_gain = jnp.matmul(gains, right_hot, precision=highest)[:, None]
    left_re, left_im = left_gain[..., 0, :], left_gain[..., 1, :]
    right_re, right_im = right_gain[..., 0, :], right_gain[..., 1, :]
    model_re, model_im = model[..., 0, :], model[..., 1, :]
    inner_re = left_re * model_re - left_im * model_im
    inner_im = left_re * model_im + left_im * model_re
    outer_re = inner_re * right_re + inner_im * right_im
    outer_im = inner_im * right_re - inner_re * right_im
    return jnp.stack([outer_re, outer_im], axis=-2), (left_re, left_im, right_re, right_im)


def solve(gains, model, corrupted_model, parts, residual, left_hot, right_hot):
    model = model.astype(jnp.float32)
    left_re, left_im, right_re, right_im = parts
    target = residual + corrupted_model
    target_re, target_im = target[..., 0, :], target[..., 1, :]
    model_re, model_im = model[..., 0, :], model[..., 1, :]
    weighted_re = target_re * model_re + target_im * model_im
    weighted_im = target_im * model_re - target_re * model_im
    left_num_re = weighted_re * right_re - weighted_im * right_im
    left_num_im = weighted_re * right_im + weighted_im * right_re
    right_num_re = weighted_re * left_re + weighted_im * left_im
    right_num_im = weighted_re * left_im - weighted_im * left_re
    power = model_re * model_re + model_im * model_im
    left_den = power * (right_re * right_re + right_im * right_im)
    right_den = power * (left_re * left_re + left_im * left_im)
    left_products = jnp.sum(jnp.stack([left_num_re, left_num_im, left_den], axis=3), axis=1)
    right_terms = jnp.sum(jnp.stack([right_num_re, right_num_im, right_den], axis=3), axis=1)
    totals = jnp.matmul(left_products, left_hot.T, precision=highest) + jnp.matmul(right_terms, right_hot.T, precision=highest)
    solved = totals[:, :, 0:2] / (totals[:, :, 2:3] + epsilon)
    return (1.0 - step_size) * gains + step_size * solved


def smooth(padded_gains, padded_weights, widths):
    count = widths.shape[0]
    half_width = widths.astype(jnp.float32) * 0.5
    numer = jnp.zeros((padded_gains.shape[0], count) + padded_gains.shape[2:], jnp.float32)
    denom = jnp.zeros((count,), jnp.float32)
    for offset in range(-SPAN, SPAN + 1):
        ratio = offset / half_width
        kernel = jnp.exp(-0.5 * ratio * ratio) * (widths >= abs(offset)).astype(jnp.float32)
        weight_here = kernel * padded_weights[SPAN + offset:SPAN + offset + count]
        numer = numer + weight_here[None, :, None, None, None] * padded_gains[:, SPAN + offset:SPAN + offset + count]
        denom = denom + weight_here
    return numer / denom[None, :, None, None, None]


def reference(visibilities, model, gains, weights, widths, baseline_table):
    left_hot, right_hot = station_tables(baseline_table)
    padded_weights = jnp.pad(weights, (SPAN, SPAN))
    current = gains
    residual = visibilities
    for sweep in range(ITERS):
        def add_dir(total, pair):
            corrupted_model, unused = corrupt(pair[0], pair[1], left_hot, right_hot)
            return total + corrupted_model, None

        zeros = jnp.zeros(visibilities.shape, jnp.float32)
        total, unused = lax.scan(add_dir, zeros, (current, model))
        residual = visibilities - total

        def one_dir(pair):
            corrupted_model, parts = corrupt(pair[0], pair[1], left_hot, right_hot)
            return solve(pair[0], pair[1], corrupted_model, parts, residual, left_hot, right_hot)

        stepped = lax.map(one_dir, (current, model))
        padded = jnp.pad(stepped, ((0, 0), (SPAN, SPAN), (0, 0), (0, 0), (0, 0)))
        current = smooth(padded, padded_weights, widths)
    return current, residual
```

```python
import jax
import jax.numpy as jnp
from jax import lax
from jax.sharding import PartitionSpec as P

STATIONS = 76
SPAN = 2
ITERS = 2


step_size = 0.6
epsilon = 1e-06
highest = lax.Precision.HIGHEST


def extended(cells, sides, width):
    for axis, dim in sides:
        count = lax.axis_size(axis)
        ends = count - 1
        head = lax.slice_in_dim(cells, 0, width, axis=dim)
        tail = lax.slice_in_dim(cells, cells.shape[dim] - width, cells.shape[dim], axis=dim)
        cells = jnp.concatenate(
            [
                lax.ppermute(tail, axis, [(i, (i + 1) % count) for i in range(ends)]),
                cells,
                lax.ppermute(head, axis, [((i + 1) % count, i) for i in range(ends)]),
            ],
            axis=dim,
        )
    return cells


def sum_over_dir(partial):
    count = lax.axis_size("dir")
    swapped = [
        lax.ppermute(partial, "dir", [(i, i ^ mask) for i in range(count)])
        for mask in (1, 2, 3)
    ]
    return (partial + swapped[0]) + (swapped[1] + swapped[2])


def station_tables(baseline_table):
    column = jnp.arange(STATIONS, dtype=jnp.int32)[:, None]
    left_hot = (baseline_table[0][None, :] == column).astype(jnp.float32)
    right_hot = (baseline_table[1][None, :] == column).astype(jnp.float32)
    return (left_hot, right_hot)


def corrupt(gains, model, left_hot, right_hot):
    model = model.astype(jnp.float32)
    left_gain = jnp.matmul(gains, left_hot, precision=highest)[:, None]
    right_gain = jnp.matmul(gains, right_hot, precision=highest)[:, None]
    left_re, left_im = (left_gain[..., 0, :], left_gain[..., 1, :])
    right_re, right_im = (right_gain[..., 0, :], right_gain[..., 1, :])
    model_re, model_im = (model[..., 0, :], model[..., 1, :])
    inner_re = left_re * model_re - left_im * model_im
    inner_im = left_re * model_im + left_im * model_re
    outer_re = inner_re * right_re + inner_im * right_im
    outer_im = inner_im * right_re - inner_re * right_im
    return (jnp.stack([outer_re, outer_im], axis=-2), (left_re, left_im, right_re, right_im))


def solve(gains, model, corrupted_model, parts, residual, left_hot, right_hot):
    model = model.astype(jnp.float32)
    left_re, left_im, right_re, right_im = parts
    target = residual + corrupted_model
    target_re, target_im = (target[..., 0, :], target[..., 1, :])
    model_re, model_im = (model[..., 0, :], model[..., 1, :])
    weighted_re = target_re * model_re + target_im * model_im
    weighted_im = target_im * model_re - target_re * model_im
    left_num_re = weighted_re * right_re - weighted_im * right_im
    left_num_im = weighted_re * right_im + weighted_im * right_re
    right_num_re = weighted_re * left_re + weighted_im * left_im
    right_num_im = weighted_re * left_im - weighted_im * left_re
    power = model_re * model_re + model_im * model_im
    left_den = power * (right_re * right_re + right_im * right_im)
    right_den = power * (left_re * left_re + left_im * left_im)
    left_products = jnp.sum(jnp.stack([left_num_re, left_num_im, left_den], axis=3), axis=1)
    right_terms = jnp.sum(jnp.stack([right_num_re, right_num_im, right_den], axis=3), axis=1)
    totals = jnp.matmul(left_products, left_hot.T, precision=highest) + jnp.matmul(
        right_terms, right_hot.T, precision=highest
    )
    solved = totals[:, :, 0:2] / (totals[:, :, 2:3] + epsilon)
    return (1.0 - step_size) * gains + step_size * solved


def smooth(padded_gains, padded_weights, widths):
    count = widths.shape[0]
    half_width = widths.astype(jnp.float32) * 0.5
    numer = jnp.zeros((padded_gains.shape[0], count) + padded_gains.shape[2:], jnp.float32)
    denom = jnp.zeros((count,), jnp.float32)
    for offset in range(-SPAN, SPAN + 1):
        ratio = offset / half_width
        kernel = jnp.exp(-0.5 * ratio * ratio) * (widths >= abs(offset)).astype(jnp.float32)
        weight_here = kernel * padded_weights[SPAN + offset : SPAN + offset + count]
        numer = (
            numer
            + weight_here[None, :, None, None, None]
            * padded_gains[:, SPAN + offset : SPAN + offset + count]
        )
        denom = denom + weight_here
    return numer / denom[None, :, None, None, None]


def on_device(visibilities, model, gains, weights, widths, baseline_table):
    left_hot, right_hot = station_tables(baseline_table)
    padded_weights = extended(weights, (("chan", 0),), SPAN)
    current = gains
    residual = visibilities
    corrupt_all = jax.vmap(corrupt, in_axes=(0, 0, None, None))
    solve_all = jax.vmap(solve, in_axes=(0, 0, 0, 0, None, None, None))
    for sweep in range(ITERS):
        corrupted_model, parts = corrupt_all(current, model, left_hot, right_hot)
        partial_total = jnp.sum(corrupted_model, axis=0)
        total = sum_over_dir(partial_total)
        residual = visibilities - total
        stepped = solve_all(current, model, corrupted_model, parts, residual, left_hot, right_hot)
        padded_gains = extended(stepped, (("chan", 1),), SPAN)
        current = smooth(padded_gains, padded_weights, widths)
    return (current, residual)


def solution(mesh):
    placed = (
        P("chan", None, None, None, None),
        P("dir", "chan", None, None, None, None),
        P("dir", "chan", None, None, None),
        P("chan"),
        P("chan"),
        P(),
    )
    return jax.shard_map(
        on_device,
        mesh=mesh,
        in_specs=placed,
        out_specs=(P("dir", "chan", None, None, None), P("chan", None, None, None, None)),
        check_vma=False,
    )
```

```python
import jax
import jax.numpy as jnp
from jax import lax
from jax.sharding import PartitionSpec as P

STATIONS = 76
SPAN = 2
ITERS = 2


step_size = 0.6
epsilon = 1e-06
highest = lax.Precision.HIGHEST


def extended(cells, sides, width):
    for axis, dim in sides:
        count = lax.axis_size(axis)
        ends = count - 1
        head = lax.slice_in_dim(cells, 0, width, axis=dim)
        tail = lax.slice_in_dim(cells, cells.shape[dim] - width, cells.shape[dim], axis=dim)
        cells = jnp.concatenate(
            [
                lax.ppermute(tail, axis, [(i, (i + 1) % count) for i in range(ends)]),
                cells,
                lax.ppermute(head, axis, [((i + 1) % count, i) for i in range(ends)]),
            ],
            axis=dim,
        )
    return cells


def sum_over_dir(partial):
    count = lax.axis_size("dir")
    total = partial
    mask = 1
    while mask < count:
        total = total + lax.ppermute(total, "dir", [(i, i ^ mask) for i in range(count)])
        mask *= 2
    return total


def station_tables(baseline_table):
    column = jnp.arange(STATIONS, dtype=jnp.int32)[:, None]
    left_hot = (baseline_table[0][None, :] == column).astype(jnp.float32)
    right_hot = (baseline_table[1][None, :] == column).astype(jnp.float32)
    return (left_hot, right_hot)


def corrupt(gains, model, left_hot, right_hot):
    model = model.astype(jnp.float32)
    left_gain = jnp.matmul(gains, left_hot, precision=highest)[:, None]
    right_gain = jnp.matmul(gains, right_hot, precision=highest)[:, None]
    left_re, left_im = (left_gain[..., 0, :], left_gain[..., 1, :])
    right_re, right_im = (right_gain[..., 0, :], right_gain[..., 1, :])
    model_re, model_im = (model[..., 0, :], model[..., 1, :])
    inner_re = left_re * model_re - left_im * model_im
    inner_im = left_re * model_im + left_im * model_re
    outer_re = inner_re * right_re + inner_im * right_im
    outer_im = inner_im * right_re - inner_re * right_im
    return (jnp.stack([outer_re, outer_im], axis=-2), (left_re, left_im, right_re, right_im))


def solve(gains, model, corrupted_model, parts, residual, left_hot, right_hot):
    model = model.astype(jnp.float32)
    left_re, left_im, right_re, right_im = parts
    target = residual + corrupted_model
    target_re, target_im = (target[..., 0, :], target[..., 1, :])
    model_re, model_im = (model[..., 0, :], model[..., 1, :])
    weighted_re = target_re * model_re + target_im * model_im
    weighted_im = target_im * model_re - target_re * model_im
    left_num_re = weighted_re * right_re - weighted_im * right_im
    left_num_im = weighted_re * right_im + weighted_im * right_re
    right_num_re = weighted_re * left_re + weighted_im * left_im
    right_num_im = weighted_re * left_im - weighted_im * left_re
    power = model_re * model_re + model_im * model_im
    left_den = power * (right_re * right_re + right_im * right_im)
    right_den = power * (left_re * left_re + left_im * left_im)
    left_products = jnp.sum(jnp.stack([left_num_re, left_num_im, left_den], axis=3), axis=1)
    right_terms = jnp.sum(jnp.stack([right_num_re, right_num_im, right_den], axis=3), axis=1)
    totals = jnp.matmul(left_products, left_hot.T, precision=highest) + jnp.matmul(
        right_terms, right_hot.T, precision=highest
    )
    solved = totals[:, :, 0:2] / (totals[:, :, 2:3] + epsilon)
    return (1.0 - step_size) * gains + step_size * solved


def smooth(padded_gains, padded_weights, widths):
    count = widths.shape[0]
    half_width = widths.astype(jnp.float32) * 0.5
    numer = jnp.zeros((padded_gains.shape[0], count) + padded_gains.shape[2:], jnp.float32)
    denom = jnp.zeros((count,), jnp.float32)
    for offset in range(-SPAN, SPAN + 1):
        ratio = offset / half_width
        kernel = jnp.exp(-0.5 * ratio * ratio) * (widths >= abs(offset)).astype(jnp.float32)
        weight_here = kernel * padded_weights[SPAN + offset : SPAN + offset + count]
        numer = (
            numer
            + weight_here[None, :, None, None, None]
            * padded_gains[:, SPAN + offset : SPAN + offset + count]
        )
        denom = denom + weight_here
    return numer / denom[None, :, None, None, None]


def on_device(visibilities, model, gains, weights, widths, baseline_table):
    left_hot, right_hot = station_tables(baseline_table)
    padded_weights = extended(weights, (("chan", 0),), SPAN)
    current = gains
    residual = visibilities
    corrupt_all = jax.vmap(corrupt, in_axes=(0, 0, None, None))
    solve_all = jax.vmap(solve, in_axes=(0, 0, 0, 0, None, None, None))
    for sweep in range(ITERS):
        corrupted_model, parts = corrupt_all(current, model, left_hot, right_hot)
        partial_total = jnp.sum(corrupted_model, axis=0)
        total = sum_over_dir(partial_total)
        residual = visibilities - total
        stepped = solve_all(current, model, corrupted_model, parts, residual, left_hot, right_hot)
        padded_gains = extended(stepped, (("chan", 1),), SPAN)
        current = smooth(padded_gains, padded_weights, widths)
    return (current, residual)


def solution(mesh):
    placed = (
        P("chan", None, None, None, None),
        P("dir", "chan", None, None, None, None),
        P("dir", "chan", None, None, None),
        P("chan"),
        P("chan"),
        P(),
    )
    return jax.shard_map(
        on_device,
        mesh=mesh,
        in_specs=placed,
        out_specs=(P("dir", "chan", None, None, None), P("chan", None, None, None, None)),
        check_vma=False,
    )
```

```python
import jax
import jax.numpy as jnp
from jax import lax
from jax.sharding import PartitionSpec as P

STATIONS = 76
SPAN = 2
ITERS = 2


step_size = 0.6
epsilon = 1e-06
highest = lax.Precision.HIGHEST


def extended(items, axis, width):
    count = lax.axis_size(axis)
    ends = count - 1

    def edge(cells, dim, first):
        size = cells.shape[dim]
        start = 0 if first else size - width
        return lax.slice_in_dim(cells, start, start + width, axis=dim)

    def send(pieces, pairs):
        flat = jnp.concatenate([piece.reshape(-1) for piece in pieces])
        arrived = lax.ppermute(flat, axis, pairs)
        out = []
        offset = 0
        for piece in pieces:
            out.append(arrived[offset : offset + piece.size].reshape(piece.shape))
            offset += piece.size
        return out

    from_left = send([edge(c, d, False) for c, d in items], [(i, i + 1) for i in range(ends)])
    from_right = send([edge(c, d, True) for c, d in items], [(i + 1, i) for i in range(ends)])
    return [
        jnp.concatenate([left, cells, right], axis=dim)
        for (cells, dim), left, right in zip(items, from_left, from_right)
    ]


def sum_over_dir(partial):
    count = lax.axis_size("dir")
    total = partial
    mask = 1
    while mask < count:
        total = total + lax.ppermute(total, "dir", [(i, i ^ mask) for i in range(count)])
        mask *= 2
    return total


def station_tables(baseline_table):
    column = jnp.arange(STATIONS, dtype=jnp.int32)[:, None]
    left_hot = (baseline_table[0][None, :] == column).astype(jnp.float32)
    right_hot = (baseline_table[1][None, :] == column).astype(jnp.float32)
    return (left_hot, right_hot)


def corrupt(gains, model, left_hot, right_hot):
    model = model.astype(jnp.float32)
    left_gain = jnp.matmul(gains, left_hot, precision=highest)[:, None]
    right_gain = jnp.matmul(gains, right_hot, precision=highest)[:, None]
    left_re, left_im = (left_gain[..., 0, :], left_gain[..., 1, :])
    right_re, right_im = (right_gain[..., 0, :], right_gain[..., 1, :])
    model_re, model_im = (model[..., 0, :], model[..., 1, :])
    inner_re = left_re * model_re - left_im * model_im
    inner_im = left_re * model_im + left_im * model_re
    outer_re = inner_re * right_re + inner_im * right_im
    outer_im = inner_im * right_re - inner_re * right_im
    return (jnp.stack([outer_re, outer_im], axis=-2), (left_re, left_im, right_re, right_im))


def solve(gains, model, corrupted_model, parts, residual, left_hot, right_hot):
    model = model.astype(jnp.float32)
    left_re, left_im, right_re, right_im = parts
    target = residual + corrupted_model
    target_re, target_im = (target[..., 0, :], target[..., 1, :])
    model_re, model_im = (model[..., 0, :], model[..., 1, :])
    weighted_re = target_re * model_re + target_im * model_im
    weighted_im = target_im * model_re - target_re * model_im
    left_num_re = weighted_re * right_re - weighted_im * right_im
    left_num_im = weighted_re * right_im + weighted_im * right_re
    right_num_re = weighted_re * left_re + weighted_im * left_im
    right_num_im = weighted_re * left_im - weighted_im * left_re
    power = model_re * model_re + model_im * model_im
    left_den = power * (right_re * right_re + right_im * right_im)
    right_den = power * (left_re * left_re + left_im * left_im)
    left_products = jnp.sum(jnp.stack([left_num_re, left_num_im, left_den], axis=3), axis=1)
    right_terms = jnp.sum(jnp.stack([right_num_re, right_num_im, right_den], axis=3), axis=1)
    totals = jnp.matmul(left_products, left_hot.T, precision=highest) + jnp.matmul(
        right_terms, right_hot.T, precision=highest
    )
    solved = totals[:, :, 0:2] / (totals[:, :, 2:3] + epsilon)
    return (1.0 - step_size) * gains + step_size * solved


def smooth(padded_gains, padded_weights, widths):
    count = widths.shape[0]
    half_width = widths.astype(jnp.float32) * 0.5
    numer = jnp.zeros((padded_gains.shape[0], count) + padded_gains.shape[2:], jnp.float32)
    denom = jnp.zeros((count,), jnp.float32)
    for offset in range(-SPAN, SPAN + 1):
        ratio = offset / half_width
        kernel = jnp.exp(-0.5 * ratio * ratio) * (widths >= abs(offset)).astype(jnp.float32)
        weight_here = kernel * padded_weights[SPAN + offset : SPAN + offset + count]
        numer = (
            numer
            + weight_here[None, :, None, None, None]
            * padded_gains[:, SPAN + offset : SPAN + offset + count]
        )
        denom = denom + weight_here
    return numer / denom[None, :, None, None, None]


def on_device(visibilities, model, gains, weights, widths, baseline_table):
    left_hot, right_hot = station_tables(baseline_table)
    padded_weights = None
    current = gains
    residual = visibilities
    corrupt_all = jax.vmap(corrupt, in_axes=(0, 0, None, None))
    solve_all = jax.vmap(solve, in_axes=(0, 0, 0, 0, None, None, None))
    for sweep in range(ITERS):
        corrupted_model, parts = corrupt_all(current, model, left_hot, right_hot)
        partial_total = jnp.sum(corrupted_model, axis=0)
        total = sum_over_dir(partial_total)
        residual = visibilities - total
        stepped = solve_all(current, model, corrupted_model, parts, residual, left_hot, right_hot)
        if padded_weights is None:
            padded_gains, padded_weights = extended(((stepped, 1), (weights, 0)), "chan", SPAN)
        else:
            (padded_gains,) = extended(((stepped, 1),), "chan", SPAN)
        current = smooth(padded_gains, padded_weights, widths)
    return (current, residual)


def solution(mesh):
    placed = (
        P("chan", None, None, None, None),
        P("dir", "chan", None, None, None, None),
        P("dir", "chan", None, None, None),
        P("chan"),
        P("chan"),
        P(),
    )
    return jax.shard_map(
        on_device,
        mesh=mesh,
        in_specs=placed,
        out_specs=(P("dir", "chan", None, None, None), P("chan", None, None, None, None)),
        check_vma=False,
    )
```

```python
import jax
import jax.numpy as jnp
from jax import lax
from jax.sharding import PartitionSpec as P

STATIONS = 76
SPAN = 2
ITERS = 2


step_size = 0.6
epsilon = 1e-06
highest = lax.Precision.HIGHEST


def extended(items, axis, width):
    count = lax.axis_size(axis)
    ends = count - 1

    def edge(cells, dim, first):
        size = cells.shape[dim]
        start = 0 if first else size - width
        return lax.slice_in_dim(cells, start, start + width, axis=dim)

    def send(pieces, pairs):
        flat = jnp.concatenate([piece.reshape(-1) for piece in pieces])
        arrived = lax.ppermute(flat, axis, pairs)
        out = []
        offset = 0
        for piece in pieces:
            out.append(arrived[offset : offset + piece.size].reshape(piece.shape))
            offset += piece.size
        return out

    from_left = send([edge(c, d, False) for c, d in items], [(i, i + 1) for i in range(ends)])
    from_right = send([edge(c, d, True) for c, d in items], [(i + 1, i) for i in range(ends)])
    return [
        jnp.concatenate([left, cells, right], axis=dim)
        for (cells, dim), left, right in zip(items, from_left, from_right)
    ]


def sum_over_dir(partial):
    count = lax.axis_size("dir")
    assert count == 4
    core = lax.axis_index("dir") % 2
    cores = [(i, i ^ 1) for i in range(count)]
    chips = [(i, i ^ 2) for i in range(count)]
    half = partial.shape[0] // 2
    low, high = partial[:half], partial[half:]
    first = core == 0
    keep = jnp.where(first, low, high)
    give = jnp.where(first, high, low)
    mine = keep + lax.ppermute(give, "dir", cores)
    owned = mine + lax.ppermute(mine, "dir", chips)
    other = lax.ppermute(owned, "dir", cores)
    return jnp.where(
        first,
        jnp.concatenate([owned, other], axis=0),
        jnp.concatenate([other, owned], axis=0),
    )


def station_tables(baseline_table):
    column = jnp.arange(STATIONS, dtype=jnp.int32)[:, None]
    left_hot = (baseline_table[0][None, :] == column).astype(jnp.float32)
    right_hot = (baseline_table[1][None, :] == column).astype(jnp.float32)
    return (left_hot, right_hot)


def corrupt(gains, model, left_hot, right_hot):
    model = model.astype(jnp.float32)
    left_gain = jnp.matmul(gains, left_hot, precision=highest)[:, None]
    right_gain = jnp.matmul(gains, right_hot, precision=highest)[:, None]
    left_re, left_im = (left_gain[..., 0, :], left_gain[..., 1, :])
    right_re, right_im = (right_gain[..., 0, :], right_gain[..., 1, :])
    model_re, model_im = (model[..., 0, :], model[..., 1, :])
    inner_re = left_re * model_re - left_im * model_im
    inner_im = left_re * model_im + left_im * model_re
    outer_re = inner_re * right_re + inner_im * right_im
    outer_im = inner_im * right_re - inner_re * right_im
    return (jnp.stack([outer_re, outer_im], axis=-2), (left_re, left_im, right_re, right_im))


def solve(gains, model, corrupted_model, parts, residual, left_hot, right_hot):
    model = model.astype(jnp.float32)
    left_re, left_im, right_re, right_im = parts
    target = residual + corrupted_model
    target_re, target_im = (target[..., 0, :], target[..., 1, :])
    model_re, model_im = (model[..., 0, :], model[..., 1, :])
    weighted_re = target_re * model_re + target_im * model_im
    weighted_im = target_im * model_re - target_re * model_im
    left_num_re = weighted_re * right_re - weighted_im * right_im
    left_num_im = weighted_re * right_im + weighted_im * right_re
    right_num_re = weighted_re * left_re + weighted_im * left_im
    right_num_im = weighted_re * left_im - weighted_im * left_re
    power = model_re * model_re + model_im * model_im
    left_den = power * (right_re * right_re + right_im * right_im)
    right_den = power * (left_re * left_re + left_im * left_im)
    left_products = jnp.sum(jnp.stack([left_num_re, left_num_im, left_den], axis=3), axis=1)
    right_terms = jnp.sum(jnp.stack([right_num_re, right_num_im, right_den], axis=3), axis=1)
    totals = jnp.matmul(left_products, left_hot.T, precision=highest) + jnp.matmul(
        right_terms, right_hot.T, precision=highest
    )
    solved = totals[:, :, 0:2] / (totals[:, :, 2:3] + epsilon)
    return (1.0 - step_size) * gains + step_size * solved


def smooth(padded_gains, padded_weights, widths):
    count = widths.shape[0]
    half_width = widths.astype(jnp.float32) * 0.5
    numer = jnp.zeros((padded_gains.shape[0], count) + padded_gains.shape[2:], jnp.float32)
    denom = jnp.zeros((count,), jnp.float32)
    for offset in range(-SPAN, SPAN + 1):
        ratio = offset / half_width
        kernel = jnp.exp(-0.5 * ratio * ratio) * (widths >= abs(offset)).astype(jnp.float32)
        weight_here = kernel * padded_weights[SPAN + offset : SPAN + offset + count]
        numer = (
            numer
            + weight_here[None, :, None, None, None]
            * padded_gains[:, SPAN + offset : SPAN + offset + count]
        )
        denom = denom + weight_here
    return numer / denom[None, :, None, None, None]


def on_device(visibilities, model, gains, weights, widths, baseline_table):
    left_hot, right_hot = station_tables(baseline_table)
    padded_weights = None
    current = gains
    residual = visibilities
    corrupt_all = jax.vmap(corrupt, in_axes=(0, 0, None, None))
    solve_all = jax.vmap(solve, in_axes=(0, 0, 0, 0, None, None, None))
    for sweep in range(ITERS):
        corrupted_model, parts = corrupt_all(current, model, left_hot, right_hot)
        partial_total = jnp.sum(corrupted_model, axis=0)
        total = sum_over_dir(partial_total)
        residual = visibilities - total
        stepped = solve_all(current, model, corrupted_model, parts, residual, left_hot, right_hot)
        if padded_weights is None:
            padded_gains, padded_weights = extended(((stepped, 1), (weights, 0)), "chan", SPAN)
        else:
            (padded_gains,) = extended(((stepped, 1),), "chan", SPAN)
        current = smooth(padded_gains, padded_weights, widths)
    return (current, residual)


def solution(mesh):
    placed = (
        P("chan", None, None, None, None),
        P("dir", "chan", None, None, None, None),
        P("dir", "chan", None, None, None),
        P("chan"),
        P("chan"),
        P(),
    )
    return jax.shard_map(
        on_device,
        mesh=mesh,
        in_specs=placed,
        out_specs=(P("dir", "chan", None, None, None), P("chan", None, None, None, None)),
        check_vma=False,
    )
```

```python
import jax
import jax.numpy as jnp
from jax import lax
from jax.sharding import PartitionSpec as P

STATIONS = 76
SPAN = 2
ITERS = 2


step_size = 0.6
epsilon = 1e-06
highest = lax.Precision.HIGHEST


def extended(items, axis, width):
    count = lax.axis_size(axis)
    ends = count - 1

    def edge(cells, dim, first):
        size = cells.shape[dim]
        start = 0 if first else size - width
        return lax.slice_in_dim(cells, start, start + width, axis=dim)

    def send(pieces, pairs):
        flat = jnp.concatenate([piece.reshape(-1) for piece in pieces])
        arrived = lax.ppermute(flat, axis, pairs)
        out = []
        offset = 0
        for piece in pieces:
            out.append(arrived[offset : offset + piece.size].reshape(piece.shape))
            offset += piece.size
        return out

    from_left = send([edge(c, d, False) for c, d in items], [(i, i + 1) for i in range(ends)])
    from_right = send([edge(c, d, True) for c, d in items], [(i + 1, i) for i in range(ends)])
    return [
        jnp.concatenate([left, cells, right], axis=dim)
        for (cells, dim), left, right in zip(items, from_left, from_right)
    ]


def sum_over_dir(partial):
    count = lax.axis_size("dir")
    spread = jnp.broadcast_to(partial[None], (count,) + partial.shape)
    parts = lax.all_to_all(spread, "dir", 0, 0)
    return (parts[0] + parts[1]) + (parts[2] + parts[3])


def station_tables(baseline_table):
    column = jnp.arange(STATIONS, dtype=jnp.int32)[:, None]
    left_hot = (baseline_table[0][None, :] == column).astype(jnp.float32)
    right_hot = (baseline_table[1][None, :] == column).astype(jnp.float32)
    return (left_hot, right_hot)


def corrupt(gains, model, left_hot, right_hot):
    model = model.astype(jnp.float32)
    left_gain = jnp.matmul(gains, left_hot, precision=highest)[:, None]
    right_gain = jnp.matmul(gains, right_hot, precision=highest)[:, None]
    left_re, left_im = (left_gain[..., 0, :], left_gain[..., 1, :])
    right_re, right_im = (right_gain[..., 0, :], right_gain[..., 1, :])
    model_re, model_im = (model[..., 0, :], model[..., 1, :])
    inner_re = left_re * model_re - left_im * model_im
    inner_im = left_re * model_im + left_im * model_re
    outer_re = inner_re * right_re + inner_im * right_im
    outer_im = inner_im * right_re - inner_re * right_im
    return (jnp.stack([outer_re, outer_im], axis=-2), (left_re, left_im, right_re, right_im))


def solve(gains, model, corrupted_model, parts, residual, left_hot, right_hot):
    model = model.astype(jnp.float32)
    left_re, left_im, right_re, right_im = parts
    target = residual + corrupted_model
    target_re, target_im = (target[..., 0, :], target[..., 1, :])
    model_re, model_im = (model[..., 0, :], model[..., 1, :])
    weighted_re = target_re * model_re + target_im * model_im
    weighted_im = target_im * model_re - target_re * model_im
    left_num_re = weighted_re * right_re - weighted_im * right_im
    left_num_im = weighted_re * right_im + weighted_im * right_re
    right_num_re = weighted_re * left_re + weighted_im * left_im
    right_num_im = weighted_re * left_im - weighted_im * left_re
    power = model_re * model_re + model_im * model_im
    left_den = power * (right_re * right_re + right_im * right_im)
    right_den = power * (left_re * left_re + left_im * left_im)
    left_products = jnp.sum(jnp.stack([left_num_re, left_num_im, left_den], axis=3), axis=1)
    right_terms = jnp.sum(jnp.stack([right_num_re, right_num_im, right_den], axis=3), axis=1)
    totals = jnp.matmul(left_products, left_hot.T, precision=highest) + jnp.matmul(
        right_terms, right_hot.T, precision=highest
    )
    solved = totals[:, :, 0:2] / (totals[:, :, 2:3] + epsilon)
    return (1.0 - step_size) * gains + step_size * solved


def smooth(padded_gains, padded_weights, widths):
    count = widths.shape[0]
    half_width = widths.astype(jnp.float32) * 0.5
    numer = jnp.zeros((padded_gains.shape[0], count) + padded_gains.shape[2:], jnp.float32)
    denom = jnp.zeros((count,), jnp.float32)
    for offset in range(-SPAN, SPAN + 1):
        ratio = offset / half_width
        kernel = jnp.exp(-0.5 * ratio * ratio) * (widths >= abs(offset)).astype(jnp.float32)
        weight_here = kernel * padded_weights[SPAN + offset : SPAN + offset + count]
        numer = (
            numer
            + weight_here[None, :, None, None, None]
            * padded_gains[:, SPAN + offset : SPAN + offset + count]
        )
        denom = denom + weight_here
    return numer / denom[None, :, None, None, None]


def on_device(visibilities, model, gains, weights, widths, baseline_table):
    left_hot, right_hot = station_tables(baseline_table)
    padded_weights = None
    current = gains
    residual = visibilities
    corrupt_all = jax.vmap(corrupt, in_axes=(0, 0, None, None))
    solve_all = jax.vmap(solve, in_axes=(0, 0, 0, 0, None, None, None))
    for sweep in range(ITERS):
        corrupted_model, parts = corrupt_all(current, model, left_hot, right_hot)
        partial_total = jnp.sum(corrupted_model, axis=0)
        total = sum_over_dir(partial_total)
        residual = visibilities - total
        stepped = solve_all(current, model, corrupted_model, parts, residual, left_hot, right_hot)
        if padded_weights is None:
            padded_gains, padded_weights = extended(((stepped, 1), (weights, 0)), "chan", SPAN)
        else:
            (padded_gains,) = extended(((stepped, 1),), "chan", SPAN)
        current = smooth(padded_gains, padded_weights, widths)
    return (current, residual)


def solution(mesh):
    placed = (
        P("chan", None, None, None, None),
        P("dir", "chan", None, None, None, None),
        P("dir", "chan", None, None, None),
        P("chan"),
        P("chan"),
        P(),
    )
    return jax.shard_map(
        on_device,
        mesh=mesh,
        in_specs=placed,
        out_specs=(P("dir", "chan", None, None, None), P("chan", None, None, None, None)),
        check_vma=False,
    )
```

```python
import jax
import jax.numpy as jnp
from jax import lax
from jax.sharding import PartitionSpec as P

STATIONS = 76
SPAN = 2
ITERS = 2


step_size = 0.6
epsilon = 1e-06
highest = lax.Precision.HIGHEST


def extended(items, axis, width):
    count = lax.axis_size(axis)
    ends = count - 1

    def edge(cells, dim, first):
        size = cells.shape[dim]
        start = 0 if first else size - width
        return lax.slice_in_dim(cells, start, start + width, axis=dim)

    def send(pieces, pairs):
        flat = jnp.concatenate([piece.reshape(-1) for piece in pieces])
        arrived = lax.ppermute(flat, axis, pairs)
        out = []
        offset = 0
        for piece in pieces:
            out.append(arrived[offset : offset + piece.size].reshape(piece.shape))
            offset += piece.size
        return out

    from_left = send([edge(c, d, False) for c, d in items], [(i, i + 1) for i in range(ends)])
    from_right = send([edge(c, d, True) for c, d in items], [(i + 1, i) for i in range(ends)])
    return [
        jnp.concatenate([left, cells, right], axis=dim)
        for (cells, dim), left, right in zip(items, from_left, from_right)
    ]


def sum_over_dir(partial):
    count = lax.axis_size("dir")
    total = partial
    mask = 1
    while mask < count:
        total = total + lax.ppermute(total, "dir", [(i, i ^ mask) for i in range(count)])
        mask *= 2
    return total


def table_dot(values, table):
    high = lax.reduce_precision(values, exponent_bits=8, mantissa_bits=7)
    rest = values - high
    middle = lax.reduce_precision(rest, exponent_bits=8, mantissa_bits=7)
    low = rest - middle
    parts = jnp.stack([high, middle, low]).astype(jnp.bfloat16)
    out = jnp.matmul(parts, table.astype(jnp.bfloat16), preferred_element_type=jnp.float32)
    return (out[0] + out[1]) + out[2]


def station_tables(baseline_table):
    column = jnp.arange(STATIONS, dtype=jnp.int32)[:, None]
    left_hot = (baseline_table[0][None, :] == column).astype(jnp.float32)
    right_hot = (baseline_table[1][None, :] == column).astype(jnp.float32)
    return (left_hot, right_hot)


def corrupt(gains, model, left_hot, right_hot):
    model = model.astype(jnp.float32)
    left_gain = table_dot(gains, left_hot)[:, None]
    right_gain = table_dot(gains, right_hot)[:, None]
    left_re, left_im = (left_gain[..., 0, :], left_gain[..., 1, :])
    right_re, right_im = (right_gain[..., 0, :], right_gain[..., 1, :])
    model_re, model_im = (model[..., 0, :], model[..., 1, :])
    inner_re = left_re * model_re - left_im * model_im
    inner_im = left_re * model_im + left_im * model_re
    outer_re = inner_re * right_re + inner_im * right_im
    outer_im = inner_im * right_re - inner_re * right_im
    return (jnp.stack([outer_re, outer_im], axis=-2), (left_re, left_im, right_re, right_im))


def solve(gains, model, corrupted_model, parts, residual, left_hot, right_hot):
    model = model.astype(jnp.float32)
    left_re, left_im, right_re, right_im = parts
    target = residual + corrupted_model
    target_re, target_im = (target[..., 0, :], target[..., 1, :])
    model_re, model_im = (model[..., 0, :], model[..., 1, :])
    weighted_re = target_re * model_re + target_im * model_im
    weighted_im = target_im * model_re - target_re * model_im
    left_num_re = weighted_re * right_re - weighted_im * right_im
    left_num_im = weighted_re * right_im + weighted_im * right_re
    right_num_re = weighted_re * left_re + weighted_im * left_im
    right_num_im = weighted_re * left_im - weighted_im * left_re
    power = model_re * model_re + model_im * model_im
    left_den = power * (right_re * right_re + right_im * right_im)
    right_den = power * (left_re * left_re + left_im * left_im)
    left_products = jnp.sum(jnp.stack([left_num_re, left_num_im, left_den], axis=3), axis=1)
    right_terms = jnp.sum(jnp.stack([right_num_re, right_num_im, right_den], axis=3), axis=1)
    totals = table_dot(left_products, left_hot.T) + table_dot(right_terms, right_hot.T)
    solved = totals[:, :, 0:2] / (totals[:, :, 2:3] + epsilon)
    return (1.0 - step_size) * gains + step_size * solved


def smooth(padded_gains, padded_weights, widths):
    count = widths.shape[0]
    half_width = widths.astype(jnp.float32) * 0.5
    numer = jnp.zeros((padded_gains.shape[0], count) + padded_gains.shape[2:], jnp.float32)
    denom = jnp.zeros((count,), jnp.float32)
    for offset in range(-SPAN, SPAN + 1):
        ratio = offset / half_width
        kernel = jnp.exp(-0.5 * ratio * ratio) * (widths >= abs(offset)).astype(jnp.float32)
        weight_here = kernel * padded_weights[SPAN + offset : SPAN + offset + count]
        numer = (
            numer
            + weight_here[None, :, None, None, None]
            * padded_gains[:, SPAN + offset : SPAN + offset + count]
        )
        denom = denom + weight_here
    return numer / denom[None, :, None, None, None]


def on_device(visibilities, model, gains, weights, widths, baseline_table):
    left_hot, right_hot = station_tables(baseline_table)
    padded_weights = None
    current = gains
    residual = visibilities
    corrupt_all = jax.vmap(corrupt, in_axes=(0, 0, None, None))
    solve_all = jax.vmap(solve, in_axes=(0, 0, 0, 0, None, None, None))
    for sweep in range(ITERS):
        corrupted_model, parts = corrupt_all(current, model, left_hot, right_hot)
        partial_total = jnp.sum(corrupted_model, axis=0)
        total = sum_over_dir(partial_total)
        residual = visibilities - total
        stepped = solve_all(current, model, corrupted_model, parts, residual, left_hot, right_hot)
        if padded_weights is None:
            padded_gains, padded_weights = extended(((stepped, 1), (weights, 0)), "chan", SPAN)
        else:
            (padded_gains,) = extended(((stepped, 1),), "chan", SPAN)
        current = smooth(padded_gains, padded_weights, widths)
    return (current, residual)


def solution(mesh):
    placed = (
        P("chan", None, None, None, None),
        P("dir", "chan", None, None, None, None),
        P("dir", "chan", None, None, None),
        P("chan"),
        P("chan"),
        P(),
    )
    return jax.shard_map(
        on_device,
        mesh=mesh,
        in_specs=placed,
        out_specs=(P("dir", "chan", None, None, None), P("chan", None, None, None, None)),
        check_vma=False,
    )
```

```python
import jax
import jax.numpy as jnp
from jax import lax
from jax.sharding import PartitionSpec as P

STATIONS = 76
SPAN = 2
ITERS = 2


step_size = 0.6
epsilon = 1e-06
highest = lax.Precision.HIGHEST


def extended(items, axis, width):
    count = lax.axis_size(axis)
    ends = count - 1

    def edge(cells, dim, first):
        size = cells.shape[dim]
        start = 0 if first else size - width
        return lax.slice_in_dim(cells, start, start + width, axis=dim)

    def send(pieces, pairs):
        flat = jnp.concatenate([piece.reshape(-1) for piece in pieces])
        arrived = lax.ppermute(flat, axis, pairs)
        out = []
        offset = 0
        for piece in pieces:
            out.append(arrived[offset : offset + piece.size].reshape(piece.shape))
            offset += piece.size
        return out

    from_left = send([edge(c, d, False) for c, d in items], [(i, i + 1) for i in range(ends)])
    from_right = send([edge(c, d, True) for c, d in items], [(i + 1, i) for i in range(ends)])
    return [
        jnp.concatenate([left, cells, right], axis=dim)
        for (cells, dim), left, right in zip(items, from_left, from_right)
    ]


def sum_over_dir(partial):
    count = lax.axis_size("dir")
    total = partial
    mask = 1
    while mask < count:
        total = total + lax.ppermute(total, "dir", [(i, i ^ mask) for i in range(count)])
        mask *= 2
    return total


def station_tables(baseline_table):
    column = jnp.arange(STATIONS, dtype=jnp.int32)[:, None]
    left_hot = (baseline_table[0][None, :] == column).astype(jnp.float32)
    right_hot = (baseline_table[1][None, :] == column).astype(jnp.float32)
    return (left_hot, right_hot)


def corrupt(gains, model, left_hot, right_hot):
    model = model.astype(jnp.float32)
    count = left_hot.shape[1]
    both = jnp.matmul(gains, jnp.concatenate([left_hot, right_hot], axis=1), precision=highest)
    left_gain = both[..., :count][:, None]
    right_gain = both[..., count:][:, None]
    left_re, left_im = (left_gain[..., 0, :], left_gain[..., 1, :])
    right_re, right_im = (right_gain[..., 0, :], right_gain[..., 1, :])
    model_re, model_im = (model[..., 0, :], model[..., 1, :])
    inner_re = left_re * model_re - left_im * model_im
    inner_im = left_re * model_im + left_im * model_re
    outer_re = inner_re * right_re + inner_im * right_im
    outer_im = inner_im * right_re - inner_re * right_im
    return (jnp.stack([outer_re, outer_im], axis=-2), (left_re, left_im, right_re, right_im))


def solve(gains, model, corrupted_model, parts, residual, left_hot, right_hot):
    model = model.astype(jnp.float32)
    left_re, left_im, right_re, right_im = parts
    target = residual + corrupted_model
    target_re, target_im = (target[..., 0, :], target[..., 1, :])
    model_re, model_im = (model[..., 0, :], model[..., 1, :])
    weighted_re = target_re * model_re + target_im * model_im
    weighted_im = target_im * model_re - target_re * model_im
    left_num_re = weighted_re * right_re - weighted_im * right_im
    left_num_im = weighted_re * right_im + weighted_im * right_re
    right_num_re = weighted_re * left_re + weighted_im * left_im
    right_num_im = weighted_re * left_im - weighted_im * left_re
    power = model_re * model_re + model_im * model_im
    left_den = power * (right_re * right_re + right_im * right_im)
    right_den = power * (left_re * left_re + left_im * left_im)
    left_products = jnp.sum(jnp.stack([left_num_re, left_num_im, left_den], axis=3), axis=1)
    right_terms = jnp.sum(jnp.stack([right_num_re, right_num_im, right_den], axis=3), axis=1)
    totals = jnp.matmul(
        jnp.concatenate([left_products, right_terms], axis=-1),
        jnp.concatenate([left_hot.T, right_hot.T], axis=0),
        precision=highest,
    )
    solved = totals[:, :, 0:2] / (totals[:, :, 2:3] + epsilon)
    return (1.0 - step_size) * gains + step_size * solved


def smooth(padded_gains, padded_weights, widths):
    count = widths.shape[0]
    half_width = widths.astype(jnp.float32) * 0.5
    numer = jnp.zeros((padded_gains.shape[0], count) + padded_gains.shape[2:], jnp.float32)
    denom = jnp.zeros((count,), jnp.float32)
    for offset in range(-SPAN, SPAN + 1):
        ratio = offset / half_width
        kernel = jnp.exp(-0.5 * ratio * ratio) * (widths >= abs(offset)).astype(jnp.float32)
        weight_here = kernel * padded_weights[SPAN + offset : SPAN + offset + count]
        numer = (
            numer
            + weight_here[None, :, None, None, None]
            * padded_gains[:, SPAN + offset : SPAN + offset + count]
        )
        denom = denom + weight_here
    return numer / denom[None, :, None, None, None]


def on_device(visibilities, model, gains, weights, widths, baseline_table):
    left_hot, right_hot = station_tables(baseline_table)
    padded_weights = None
    current = gains
    residual = visibilities
    corrupt_all = jax.vmap(corrupt, in_axes=(0, 0, None, None))
    solve_all = jax.vmap(solve, in_axes=(0, 0, 0, 0, None, None, None))
    for sweep in range(ITERS):
        corrupted_model, parts = corrupt_all(current, model, left_hot, right_hot)
        partial_total = jnp.sum(corrupted_model, axis=0)
        total = sum_over_dir(partial_total)
        residual = visibilities - total
        stepped = solve_all(current, model, corrupted_model, parts, residual, left_hot, right_hot)
        if padded_weights is None:
            padded_gains, padded_weights = extended(((stepped, 1), (weights, 0)), "chan", SPAN)
        else:
            (padded_gains,) = extended(((stepped, 1),), "chan", SPAN)
        current = smooth(padded_gains, padded_weights, widths)
    return (current, residual)


def solution(mesh):
    placed = (
        P("chan", None, None, None, None),
        P("dir", "chan", None, None, None, None),
        P("dir", "chan", None, None, None),
        P("chan"),
        P("chan"),
        P(),
    )
    return jax.shard_map(
        on_device,
        mesh=mesh,
        in_specs=placed,
        out_specs=(P("dir", "chan", None, None, None), P("chan", None, None, None, None)),
        check_vma=False,
    )
```

```python
import jax
import jax.numpy as jnp
from jax import lax
from jax.sharding import PartitionSpec as P

STATIONS = 76
SPAN = 2
ITERS = 2


step_size = 0.6
epsilon = 1e-06
highest = lax.Precision.HIGHEST


def extended(items, axis, width):
    count = lax.axis_size(axis)
    ends = count - 1

    def edge(cells, dim, first):
        size = cells.shape[dim]
        start = 0 if first else size - width
        return lax.slice_in_dim(cells, start, start + width, axis=dim)

    def send(pieces, pairs):
        flat = jnp.concatenate([piece.reshape(-1) for piece in pieces])
        arrived = lax.ppermute(flat, axis, pairs)
        out = []
        offset = 0
        for piece in pieces:
            out.append(arrived[offset : offset + piece.size].reshape(piece.shape))
            offset += piece.size
        return out

    from_left = send([edge(c, d, False) for c, d in items], [(i, i + 1) for i in range(ends)])
    from_right = send([edge(c, d, True) for c, d in items], [(i + 1, i) for i in range(ends)])
    return [
        jnp.concatenate([left, cells, right], axis=dim)
        for (cells, dim), left, right in zip(items, from_left, from_right)
    ]


def sum_over_dir(partial):
    count = lax.axis_size("dir")
    total = partial
    mask = 1
    while mask < count:
        total = total + lax.ppermute(total, "dir", [(i, i ^ mask) for i in range(count)])
        mask *= 2
    return total


def station_tables(baseline_table):
    column = jnp.arange(STATIONS, dtype=jnp.int32)[:, None]
    hot = (baseline_table[:, None, :] == column[None]).astype(jnp.float32)
    return (hot[0], hot[1])


def corrupt(gains, model, left_hot, right_hot):
    model = model.astype(jnp.float32)
    left_gain = jnp.matmul(gains, left_hot, precision=highest)[:, None]
    right_gain = jnp.matmul(gains, right_hot, precision=highest)[:, None]
    left_re, left_im = (left_gain[..., 0, :], left_gain[..., 1, :])
    right_re, right_im = (right_gain[..., 0, :], right_gain[..., 1, :])
    model_re, model_im = (model[..., 0, :], model[..., 1, :])
    inner_re = left_re * model_re - left_im * model_im
    inner_im = left_re * model_im + left_im * model_re
    outer_re = inner_re * right_re + inner_im * right_im
    outer_im = inner_im * right_re - inner_re * right_im
    return (jnp.stack([outer_re, outer_im], axis=-2), (left_re, left_im, right_re, right_im))


def solve(gains, model, corrupted_model, parts, residual, left_hot, right_hot):
    model = model.astype(jnp.float32)
    left_re, left_im, right_re, right_im = parts
    target = residual + corrupted_model
    target_re, target_im = (target[..., 0, :], target[..., 1, :])
    model_re, model_im = (model[..., 0, :], model[..., 1, :])
    weighted_re = target_re * model_re + target_im * model_im
    weighted_im = target_im * model_re - target_re * model_im
    left_num_re = weighted_re * right_re - weighted_im * right_im
    left_num_im = weighted_re * right_im + weighted_im * right_re
    right_num_re = weighted_re * left_re + weighted_im * left_im
    right_num_im = weighted_re * left_im - weighted_im * left_re
    power = model_re * model_re + model_im * model_im
    left_den = power * (right_re * right_re + right_im * right_im)
    right_den = power * (left_re * left_re + left_im * left_im)
    left_products = jnp.sum(jnp.stack([left_num_re, left_num_im, left_den], axis=3), axis=1)
    right_terms = jnp.sum(jnp.stack([right_num_re, right_num_im, right_den], axis=3), axis=1)
    totals = jnp.matmul(left_products, left_hot.T, precision=highest) + jnp.matmul(
        right_terms, right_hot.T, precision=highest
    )
    solved = totals[:, :, 0:2] / (totals[:, :, 2:3] + epsilon)
    return (1.0 - step_size) * gains + step_size * solved


def smooth(padded_gains, padded_weights, widths):
    count = widths.shape[0]
    half_width = widths.astype(jnp.float32) * 0.5
    numer = jnp.zeros((padded_gains.shape[0], count) + padded_gains.shape[2:], jnp.float32)
    denom = jnp.zeros((count,), jnp.float32)
    for offset in range(-SPAN, SPAN + 1):
        ratio = offset / half_width
        kernel = jnp.exp(-0.5 * ratio * ratio) * (widths >= abs(offset)).astype(jnp.float32)
        weight_here = kernel * padded_weights[SPAN + offset : SPAN + offset + count]
        numer = (
            numer
            + weight_here[None, :, None, None, None]
            * padded_gains[:, SPAN + offset : SPAN + offset + count]
        )
        denom = denom + weight_here
    return numer / denom[None, :, None, None, None]


def on_device(visibilities, model, gains, weights, widths, baseline_table):
    left_hot, right_hot = station_tables(baseline_table)
    padded_weights = None
    current = gains
    residual = visibilities
    corrupt_all = jax.vmap(corrupt, in_axes=(0, 0, None, None))
    solve_all = jax.vmap(solve, in_axes=(0, 0, 0, 0, None, None, None))
    for sweep in range(ITERS):
        corrupted_model, parts = corrupt_all(current, model, left_hot, right_hot)
        partial_total = jnp.sum(corrupted_model, axis=0)
        total = sum_over_dir(partial_total)
        residual = visibilities - total
        stepped = solve_all(current, model, corrupted_model, parts, residual, left_hot, right_hot)
        if padded_weights is None:
            padded_gains, padded_weights = extended(((stepped, 1), (weights, 0)), "chan", SPAN)
        else:
            (padded_gains,) = extended(((stepped, 1),), "chan", SPAN)
        current = smooth(padded_gains, padded_weights, widths)
    return (current, residual)


def solution(mesh):
    placed = (
        P("chan", None, None, None, None),
        P("dir", "chan", None, None, None, None),
        P("dir", "chan", None, None, None),
        P("chan"),
        P("chan"),
        P(),
    )
    return jax.shard_map(
        on_device,
        mesh=mesh,
        in_specs=placed,
        out_specs=(P("dir", "chan", None, None, None), P("chan", None, None, None, None)),
        check_vma=False,
    )
```

```python
import jax
import jax.numpy as jnp
from jax import lax
from jax.sharding import PartitionSpec as P

STATIONS = 76
SPAN = 2
ITERS = 2


step_size = 0.6
epsilon = 1e-06
table_precision = lax.Precision.HIGH


def extended(items, axis, width):
    count = lax.axis_size(axis)
    ends = count - 1

    def edge(cells, dim, first):
        size = cells.shape[dim]
        start = 0 if first else size - width
        return lax.slice_in_dim(cells, start, start + width, axis=dim)

    def send(pieces, pairs):
        flat = jnp.concatenate([piece.reshape(-1) for piece in pieces])
        arrived = lax.ppermute(flat, axis, pairs)
        out = []
        offset = 0
        for piece in pieces:
            out.append(arrived[offset : offset + piece.size].reshape(piece.shape))
            offset += piece.size
        return out

    from_left = send([edge(c, d, False) for c, d in items], [(i, i + 1) for i in range(ends)])
    from_right = send([edge(c, d, True) for c, d in items], [(i + 1, i) for i in range(ends)])
    return [
        jnp.concatenate([left, cells, right], axis=dim)
        for (cells, dim), left, right in zip(items, from_left, from_right)
    ]


def sum_over_dir(partial):
    count = lax.axis_size("dir")
    total = partial
    mask = 1
    while mask < count:
        total = total + lax.ppermute(total, "dir", [(i, i ^ mask) for i in range(count)])
        mask *= 2
    return total


def station_tables(baseline_table):
    column = jnp.arange(STATIONS, dtype=jnp.int32)[:, None]
    left_hot = (baseline_table[0][None, :] == column).astype(jnp.float32)
    right_hot = (baseline_table[1][None, :] == column).astype(jnp.float32)
    return (left_hot, right_hot)


def corrupt(gains, model, left_hot, right_hot):
    model = model.astype(jnp.float32)
    left_gain = jnp.matmul(gains, left_hot, precision=table_precision)[:, None]
    right_gain = jnp.matmul(gains, right_hot, precision=table_precision)[:, None]
    left_re, left_im = (left_gain[..., 0, :], left_gain[..., 1, :])
    right_re, right_im = (right_gain[..., 0, :], right_gain[..., 1, :])
    model_re, model_im = (model[..., 0, :], model[..., 1, :])
    inner_re = left_re * model_re - left_im * model_im
    inner_im = left_re * model_im + left_im * model_re
    outer_re = inner_re * right_re + inner_im * right_im
    outer_im = inner_im * right_re - inner_re * right_im
    return (jnp.stack([outer_re, outer_im], axis=-2), (left_re, left_im, right_re, right_im))


def solve(gains, model, corrupted_model, parts, residual, left_hot, right_hot):
    model = model.astype(jnp.float32)
    left_re, left_im, right_re, right_im = parts
    target = residual + corrupted_model
    target_re, target_im = (target[..., 0, :], target[..., 1, :])
    model_re, model_im = (model[..., 0, :], model[..., 1, :])
    weighted_re = target_re * model_re + target_im * model_im
    weighted_im = target_im * model_re - target_re * model_im
    left_num_re = weighted_re * right_re - weighted_im * right_im
    left_num_im = weighted_re * right_im + weighted_im * right_re
    right_num_re = weighted_re * left_re + weighted_im * left_im
    right_num_im = weighted_re * left_im - weighted_im * left_re
    power = model_re * model_re + model_im * model_im
    left_den = power * (right_re * right_re + right_im * right_im)
    right_den = power * (left_re * left_re + left_im * left_im)
    left_products = jnp.sum(jnp.stack([left_num_re, left_num_im, left_den], axis=3), axis=1)
    right_terms = jnp.sum(jnp.stack([right_num_re, right_num_im, right_den], axis=3), axis=1)
    totals = jnp.matmul(left_products, left_hot.T, precision=table_precision) + jnp.matmul(
        right_terms, right_hot.T, precision=table_precision
    )
    solved = totals[:, :, 0:2] / (totals[:, :, 2:3] + epsilon)
    return (1.0 - step_size) * gains + step_size * solved


def smooth(padded_gains, padded_weights, widths):
    count = widths.shape[0]
    half_width = widths.astype(jnp.float32) * 0.5
    numer = jnp.zeros((padded_gains.shape[0], count) + padded_gains.shape[2:], jnp.float32)
    denom = jnp.zeros((count,), jnp.float32)
    for offset in range(-SPAN, SPAN + 1):
        ratio = offset / half_width
        kernel = jnp.exp(-0.5 * ratio * ratio) * (widths >= abs(offset)).astype(jnp.float32)
        weight_here = kernel * padded_weights[SPAN + offset : SPAN + offset + count]
        numer = (
            numer
            + weight_here[None, :, None, None, None]
            * padded_gains[:, SPAN + offset : SPAN + offset + count]
        )
        denom = denom + weight_here
    return numer / denom[None, :, None, None, None]


def on_device(visibilities, model, gains, weights, widths, baseline_table):
    left_hot, right_hot = station_tables(baseline_table)
    padded_weights = None
    current = gains
    residual = visibilities
    corrupt_all = jax.vmap(corrupt, in_axes=(0, 0, None, None))
    solve_all = jax.vmap(solve, in_axes=(0, 0, 0, 0, None, None, None))
    for sweep in range(ITERS):
        corrupted_model, parts = corrupt_all(current, model, left_hot, right_hot)
        partial_total = jnp.sum(corrupted_model, axis=0)
        total = sum_over_dir(partial_total)
        residual = visibilities - total
        stepped = solve_all(current, model, corrupted_model, parts, residual, left_hot, right_hot)
        if padded_weights is None:
            padded_gains, padded_weights = extended(((stepped, 1), (weights, 0)), "chan", SPAN)
        else:
            (padded_gains,) = extended(((stepped, 1),), "chan", SPAN)
        current = smooth(padded_gains, padded_weights, widths)
    return (current, residual)


def solution(mesh):
    placed = (
        P("chan", None, None, None, None),
        P("dir", "chan", None, None, None, None),
        P("dir", "chan", None, None, None),
        P("chan"),
        P("chan"),
        P(),
    )
    return jax.shard_map(
        on_device,
        mesh=mesh,
        in_specs=placed,
        out_specs=(P("dir", "chan", None, None, None), P("chan", None, None, None, None)),
        check_vma=False,
    )
```

```python
import jax
import jax.numpy as jnp
from jax import lax
from jax.sharding import PartitionSpec as P

STATIONS = 76
SPAN = 2
ITERS = 2


step_size = 0.6
epsilon = 1e-06
table_precision = lax.Precision.HIGH


def extended(cells, axis, dim, width):
    count = lax.axis_size(axis)
    ends = count - 1
    size = cells.shape[dim]
    head = lax.slice_in_dim(cells, 0, width, axis=dim)
    tail = lax.slice_in_dim(cells, size - width, size, axis=dim)
    return jnp.concatenate(
        [
            lax.ppermute(tail, axis, [(i, i + 1) for i in range(ends)]),
            cells,
            lax.ppermute(head, axis, [(i + 1, i) for i in range(ends)]),
        ],
        axis=dim,
    )


def sum_over_dir(partial):
    count = lax.axis_size("dir")
    total = partial
    mask = 1
    while mask < count:
        total = total + lax.ppermute(total, "dir", [(i, i ^ mask) for i in range(count)])
        mask *= 2
    return total


def station_tables(baseline_table):
    column = jnp.arange(STATIONS, dtype=jnp.int32)[:, None]
    left_hot = (baseline_table[0][None, :] == column).astype(jnp.float32)
    right_hot = (baseline_table[1][None, :] == column).astype(jnp.float32)
    return (left_hot, right_hot)


def corrupt(gains, model, left_hot, right_hot):
    model = model.astype(jnp.float32)
    left_gain = jnp.matmul(gains, left_hot, precision=table_precision)[:, None]
    right_gain = jnp.matmul(gains, right_hot, precision=table_precision)[:, None]
    left_re, left_im = (left_gain[..., 0, :], left_gain[..., 1, :])
    right_re, right_im = (right_gain[..., 0, :], right_gain[..., 1, :])
    model_re, model_im = (model[..., 0, :], model[..., 1, :])
    inner_re = left_re * model_re - left_im * model_im
    inner_im = left_re * model_im + left_im * model_re
    outer_re = inner_re * right_re + inner_im * right_im
    outer_im = inner_im * right_re - inner_re * right_im
    return (jnp.stack([outer_re, outer_im], axis=-2), (left_re, left_im, right_re, right_im))


def solve(gains, model, corrupted_model, parts, residual, left_hot, right_hot):
    model = model.astype(jnp.float32)
    left_re, left_im, right_re, right_im = parts
    target = residual + corrupted_model
    target_re, target_im = (target[..., 0, :], target[..., 1, :])
    model_re, model_im = (model[..., 0, :], model[..., 1, :])
    weighted_re = target_re * model_re + target_im * model_im
    weighted_im = target_im * model_re - target_re * model_im
    left_num_re = weighted_re * right_re - weighted_im * right_im
    left_num_im = weighted_re * right_im + weighted_im * right_re
    right_num_re = weighted_re * left_re + weighted_im * left_im
    right_num_im = weighted_re * left_im - weighted_im * left_re
    power = model_re * model_re + model_im * model_im
    left_den = power * (right_re * right_re + right_im * right_im)
    right_den = power * (left_re * left_re + left_im * left_im)
    left_products = jnp.sum(jnp.stack([left_num_re, left_num_im, left_den], axis=3), axis=1)
    right_terms = jnp.sum(jnp.stack([right_num_re, right_num_im, right_den], axis=3), axis=1)
    totals = jnp.matmul(left_products, left_hot.T, precision=table_precision) + jnp.matmul(
        right_terms, right_hot.T, precision=table_precision
    )
    solved = totals[:, :, 0:2] / (totals[:, :, 2:3] + epsilon)
    return (1.0 - step_size) * gains + step_size * solved


def smooth(padded_gains, padded_weights, widths):
    count = widths.shape[0]
    half_width = widths.astype(jnp.float32) * 0.5
    numer = jnp.zeros((padded_gains.shape[0], count) + padded_gains.shape[2:], jnp.float32)
    denom = jnp.zeros((count,), jnp.float32)
    for offset in range(-SPAN, SPAN + 1):
        ratio = offset / half_width
        kernel = jnp.exp(-0.5 * ratio * ratio) * (widths >= abs(offset)).astype(jnp.float32)
        weight_here = kernel * padded_weights[SPAN + offset : SPAN + offset + count]
        numer = (
            numer
            + weight_here[None, :, None, None, None]
            * padded_gains[:, SPAN + offset : SPAN + offset + count]
        )
        denom = denom + weight_here
    return numer / denom[None, :, None, None, None]


def on_device(visibilities, model, gains, weights, widths, baseline_table):
    left_hot, right_hot = station_tables(baseline_table)
    padded_weights = None
    current = gains
    residual = visibilities
    corrupt_all = jax.vmap(corrupt, in_axes=(0, 0, None, None))
    solve_all = jax.vmap(solve, in_axes=(0, 0, 0, 0, None, None, None))
    for sweep in range(ITERS):
        corrupted_model, parts = corrupt_all(current, model, left_hot, right_hot)
        partial_total = jnp.sum(corrupted_model, axis=0)
        total = sum_over_dir(partial_total)
        residual = visibilities - total
        stepped = solve_all(current, model, corrupted_model, parts, residual, left_hot, right_hot)
        if padded_weights is None:
            column = jnp.broadcast_to(weights[None, :, None, None, None], stepped.shape[:-1] + (1,))
            padded = extended(jnp.concatenate([stepped, column], axis=-1), "chan", 1, SPAN)
            padded_gains = padded[..., :-1]
            padded_weights = padded[0, :, 0, 0, -1]
        else:
            padded_gains = extended(stepped, "chan", 1, SPAN)
        current = smooth(padded_gains, padded_weights, widths)
    return (current, residual)


def solution(mesh):
    placed = (
        P("chan", None, None, None, None),
        P("dir", "chan", None, None, None, None),
        P("dir", "chan", None, None, None),
        P("chan"),
        P("chan"),
        P(),
    )
    return jax.shard_map(
        on_device,
        mesh=mesh,
        in_specs=placed,
        out_specs=(P("dir", "chan", None, None, None), P("chan", None, None, None, None)),
        check_vma=False,
    )
```

```python
import jax
import jax.numpy as jnp
from jax import lax
from jax.sharding import PartitionSpec as P

STATIONS = 76
SPAN = 2
ITERS = 2


step_size = 0.6
epsilon = 1e-06
table_precision = lax.Precision.HIGH


def extended(cells, axis, dim, width):
    count = lax.axis_size(axis)
    ends = count - 1
    size = cells.shape[dim]
    head = lax.slice_in_dim(cells, 0, width, axis=dim)
    tail = lax.slice_in_dim(cells, size - width, size, axis=dim)
    return jnp.concatenate(
        [
            lax.ppermute(tail, axis, [(i, i + 1) for i in range(ends)]),
            cells,
            lax.ppermute(head, axis, [(i + 1, i) for i in range(ends)]),
        ],
        axis=dim,
    )


def sum_over_dir(partial):
    count = lax.axis_size("dir")
    total = partial
    mask = 1
    while mask < count:
        total = total + lax.ppermute(total, "dir", [(i, i ^ mask) for i in range(count)])
        mask *= 2
    return total


def station_tables(baseline_table):
    column = jnp.arange(STATIONS, dtype=jnp.int32)[:, None]
    left_hot = (baseline_table[0][None, :] == column).astype(jnp.float32)
    right_hot = (baseline_table[1][None, :] == column).astype(jnp.float32)
    return (left_hot, right_hot)


def corrupt(gains, model, left_hot, right_hot):
    model = model.astype(jnp.float32)
    left_gain = jnp.matmul(gains, left_hot, precision=table_precision)[:, None]
    right_gain = jnp.matmul(gains, right_hot, precision=table_precision)[:, None]
    left_re, left_im = (left_gain[..., 0, :], left_gain[..., 1, :])
    right_re, right_im = (right_gain[..., 0, :], right_gain[..., 1, :])
    model_re, model_im = (model[..., 0, :], model[..., 1, :])
    inner_re = left_re * model_re - left_im * model_im
    inner_im = left_re * model_im + left_im * model_re
    outer_re = inner_re * right_re + inner_im * right_im
    outer_im = inner_im * right_re - inner_re * right_im
    return (jnp.stack([outer_re, outer_im], axis=-2), (left_re, left_im, right_re, right_im))


def solve(gains, model, corrupted_model, parts, visibilities, total, left_hot, right_hot):
    model = model.astype(jnp.float32)
    left_re, left_im, right_re, right_im = parts
    target = visibilities + (corrupted_model - total)
    target_re, target_im = (target[..., 0, :], target[..., 1, :])
    model_re, model_im = (model[..., 0, :], model[..., 1, :])
    weighted_re = target_re * model_re + target_im * model_im
    weighted_im = target_im * model_re - target_re * model_im
    left_num_re = weighted_re * right_re - weighted_im * right_im
    left_num_im = weighted_re * right_im + weighted_im * right_re
    right_num_re = weighted_re * left_re + weighted_im * left_im
    right_num_im = weighted_re * left_im - weighted_im * left_re
    power = model_re * model_re + model_im * model_im
    left_den = power * (right_re * right_re + right_im * right_im)
    right_den = power * (left_re * left_re + left_im * left_im)
    left_products = jnp.sum(jnp.stack([left_num_re, left_num_im, left_den], axis=3), axis=1)
    right_terms = jnp.sum(jnp.stack([right_num_re, right_num_im, right_den], axis=3), axis=1)
    totals = jnp.matmul(left_products, left_hot.T, precision=table_precision) + jnp.matmul(
        right_terms, right_hot.T, precision=table_precision
    )
    solved = totals[:, :, 0:2] / (totals[:, :, 2:3] + epsilon)
    return (1.0 - step_size) * gains + step_size * solved


def smooth(padded_gains, padded_weights, widths):
    count = widths.shape[0]
    half_width = widths.astype(jnp.float32) * 0.5
    numer = jnp.zeros((padded_gains.shape[0], count) + padded_gains.shape[2:], jnp.float32)
    denom = jnp.zeros((count,), jnp.float32)
    for offset in range(-SPAN, SPAN + 1):
        ratio = offset / half_width
        kernel = jnp.exp(-0.5 * ratio * ratio) * (widths >= abs(offset)).astype(jnp.float32)
        weight_here = kernel * padded_weights[SPAN + offset : SPAN + offset + count]
        numer = (
            numer
            + weight_here[None, :, None, None, None]
            * padded_gains[:, SPAN + offset : SPAN + offset + count]
        )
        denom = denom + weight_here
    return numer / denom[None, :, None, None, None]


def on_device(visibilities, model, gains, weights, widths, baseline_table):
    left_hot, right_hot = station_tables(baseline_table)
    padded_weights = None
    current = gains
    residual = visibilities
    corrupt_all = jax.vmap(corrupt, in_axes=(0, 0, None, None))
    solve_all = jax.vmap(solve, in_axes=(0, 0, 0, 0, None, None, None, None))
    for sweep in range(ITERS):
        corrupted_model, parts = corrupt_all(current, model, left_hot, right_hot)
        partial_total = jnp.sum(corrupted_model, axis=0)
        total = sum_over_dir(partial_total)
        residual = visibilities - total
        stepped = solve_all(current, model, corrupted_model, parts, visibilities, total, left_hot, right_hot)
        if padded_weights is None:
            column = jnp.broadcast_to(weights[None, :, None, None, None], stepped.shape[:-1] + (1,))
            padded = extended(jnp.concatenate([stepped, column], axis=-1), "chan", 1, SPAN)
            padded_gains = padded[..., :-1]
            padded_weights = padded[0, :, 0, 0, -1]
        else:
            padded_gains = extended(stepped, "chan", 1, SPAN)
        current = smooth(padded_gains, padded_weights, widths)
    return (current, residual)


def solution(mesh):
    placed = (
        P("chan", None, None, None, None),
        P("dir", "chan", None, None, None, None),
        P("dir", "chan", None, None, None),
        P("chan"),
        P("chan"),
        P(),
    )
    return jax.shard_map(
        on_device,
        mesh=mesh,
        in_specs=placed,
        out_specs=(P("dir", "chan", None, None, None), P("chan", None, None, None, None)),
        check_vma=False,
    )
```

```python
import jax
import jax.numpy as jnp
from jax import lax
from jax.sharding import PartitionSpec as P

STATIONS = 76
SPAN = 2
ITERS = 2


step_size = 0.6
epsilon = 1e-06
table_precision = lax.Precision.HIGHEST


def extended(cells, axis, dim, width):
    count = lax.axis_size(axis)
    ends = count - 1
    size = cells.shape[dim]
    head = lax.slice_in_dim(cells, 0, width, axis=dim)
    tail = lax.slice_in_dim(cells, size - width, size, axis=dim)
    return jnp.concatenate(
        [
            lax.ppermute(tail, axis, [(i, i + 1) for i in range(ends)]),
            cells,
            lax.ppermute(head, axis, [(i + 1, i) for i in range(ends)]),
        ],
        axis=dim,
    )


def sum_over_dir(partial):
    count = lax.axis_size("dir")
    total = partial
    mask = 1
    while mask < count:
        total = total + lax.ppermute(total, "dir", [(i, i ^ mask) for i in range(count)])
        mask *= 2
    return total


def station_tables(baseline_table):
    column = jnp.arange(STATIONS, dtype=jnp.int32)[:, None]
    left_hot = (baseline_table[0][None, :] == column).astype(jnp.float32)
    right_hot = (baseline_table[1][None, :] == column).astype(jnp.float32)
    return (left_hot, right_hot)


def corrupt(gains, model, left_hot, right_hot):
    model = model.astype(jnp.float32)
    left_gain = jnp.matmul(gains, left_hot, precision=table_precision)[:, None]
    right_gain = jnp.matmul(gains, right_hot, precision=table_precision)[:, None]
    left_re, left_im = (left_gain[..., 0, :], left_gain[..., 1, :])
    right_re, right_im = (right_gain[..., 0, :], right_gain[..., 1, :])
    model_re, model_im = (model[..., 0, :], model[..., 1, :])
    inner_re = left_re * model_re - left_im * model_im
    inner_im = left_re * model_im + left_im * model_re
    outer_re = inner_re * right_re + inner_im * right_im
    outer_im = inner_im * right_re - inner_re * right_im
    return (jnp.stack([outer_re, outer_im], axis=-2), (left_re, left_im, right_re, right_im))


def solve(gains, model, corrupted_model, parts, residual, left_hot, right_hot):
    model = model.astype(jnp.float32)
    left_re, left_im, right_re, right_im = parts
    target = residual + corrupted_model
    target_re, target_im = (target[..., 0, :], target[..., 1, :])
    model_re, model_im = (model[..., 0, :], model[..., 1, :])
    weighted_re = target_re * model_re + target_im * model_im
    weighted_im = target_im * model_re - target_re * model_im
    left_num_re = weighted_re * right_re - weighted_im * right_im
    left_num_im = weighted_re * right_im + weighted_im * right_re
    right_num_re = weighted_re * left_re + weighted_im * left_im
    right_num_im = weighted_re * left_im - weighted_im * left_re
    power = model_re * model_re + model_im * model_im
    left_den = power * (right_re * right_re + right_im * right_im)
    right_den = power * (left_re * left_re + left_im * left_im)
    left_products = jnp.sum(jnp.stack([left_num_re, left_num_im, left_den], axis=3), axis=1)
    right_terms = jnp.sum(jnp.stack([right_num_re, right_num_im, right_den], axis=3), axis=1)
    totals = jnp.matmul(left_products, left_hot.T, precision=table_precision) + jnp.matmul(
        right_terms, right_hot.T, precision=table_precision
    )
    solved = totals[:, :, 0:2] / (totals[:, :, 2:3] + epsilon)
    return (1.0 - step_size) * gains + step_size * solved


def smooth(padded_gains, padded_weights, widths):
    count = widths.shape[0]
    half_width = widths.astype(jnp.float32) * 0.5
    numer = jnp.zeros((padded_gains.shape[0], count) + padded_gains.shape[2:], jnp.float32)
    denom = jnp.zeros((count,), jnp.float32)
    for offset in range(-SPAN, SPAN + 1):
        ratio = offset / half_width
        kernel = jnp.exp(-0.5 * ratio * ratio) * (widths >= abs(offset)).astype(jnp.float32)
        weight_here = kernel * padded_weights[SPAN + offset : SPAN + offset + count]
        numer = (
            numer
            + weight_here[None, :, None, None, None]
            * padded_gains[:, SPAN + offset : SPAN + offset + count]
        )
        denom = denom + weight_here
    return numer / denom[None, :, None, None, None]


def on_device(visibilities, model, gains, weights, widths, baseline_table):
    left_hot, right_hot = station_tables(baseline_table)
    padded_weights = None
    current = gains
    residual = visibilities
    corrupt_all = jax.vmap(corrupt, in_axes=(0, 0, None, None))
    solve_all = jax.vmap(solve, in_axes=(0, 0, 0, 0, None, None, None))
    for sweep in range(ITERS):
        corrupted_model, parts = corrupt_all(current, model, left_hot, right_hot)
        partial_total = jnp.sum(corrupted_model, axis=0)
        total = sum_over_dir(partial_total)
        residual = visibilities - total
        stepped = solve_all(current, model, corrupted_model, parts, residual, left_hot, right_hot)
        if padded_weights is None:
            column = jnp.broadcast_to(weights[None, :, None, None, None], stepped.shape[:-1] + (1,))
            padded = extended(jnp.concatenate([stepped, column], axis=-1), "chan", 1, SPAN)
            padded_gains = padded[..., :-1]
            padded_weights = padded[0, :, 0, 0, -1]
        else:
            padded_gains = extended(stepped, "chan", 1, SPAN)
        current = smooth(padded_gains, padded_weights, widths)
    return (current, residual)


def solution(mesh):
    placed = (
        P("chan", None, None, None, None),
        P("dir", "chan", None, None, None, None),
        P("dir", "chan", None, None, None),
        P("chan"),
        P("chan"),
        P(),
    )
    return jax.shard_map(
        on_device,
        mesh=mesh,
        in_specs=placed,
        out_specs=(P("dir", "chan", None, None, None), P("chan", None, None, None, None)),
        check_vma=False,
    )
```

```python
import jax
import jax.numpy as jnp
from jax import lax
from jax.sharding import PartitionSpec as P

STATIONS = 76
SPAN = 2
ITERS = 2


step_size = 0.6
epsilon = 1e-06


def extended(cells, axis, dim, width):
    count = lax.axis_size(axis)
    ends = count - 1
    size = cells.shape[dim]
    head = lax.slice_in_dim(cells, 0, width, axis=dim)
    tail = lax.slice_in_dim(cells, size - width, size, axis=dim)
    return jnp.concatenate(
        [
            lax.ppermute(tail, axis, [(i, i + 1) for i in range(ends)]),
            cells,
            lax.ppermute(head, axis, [(i + 1, i) for i in range(ends)]),
        ],
        axis=dim,
    )


def sum_over_dir(partial):
    count = lax.axis_size("dir")
    total = partial
    mask = 1
    while mask < count:
        total = total + lax.ppermute(total, "dir", [(i, i ^ mask) for i in range(count)])
        mask *= 2
    return total


def table_dot(values, table):
    high = lax.reduce_precision(values, exponent_bits=8, mantissa_bits=7)
    parts = jnp.stack([high, values - high])
    out = jnp.matmul(parts, table, precision=lax.Precision.HIGH)
    return out[0] + out[1]


def station_tables(baseline_table):
    column = jnp.arange(STATIONS, dtype=jnp.int32)[:, None]
    left_hot = (baseline_table[0][None, :] == column).astype(jnp.float32)
    right_hot = (baseline_table[1][None, :] == column).astype(jnp.float32)
    return (left_hot, right_hot)


def corrupt(gains, model, left_hot, right_hot):
    model = model.astype(jnp.float32)
    left_gain = table_dot(gains, left_hot)[:, None]
    right_gain = table_dot(gains, right_hot)[:, None]
    left_re, left_im = (left_gain[..., 0, :], left_gain[..., 1, :])
    right_re, right_im = (right_gain[..., 0, :], right_gain[..., 1, :])
    model_re, model_im = (model[..., 0, :], model[..., 1, :])
    inner_re = left_re * model_re - left_im * model_im
    inner_im = left_re * model_im + left_im * model_re
    outer_re = inner_re * right_re + inner_im * right_im
    outer_im = inner_im * right_re - inner_re * right_im
    return (jnp.stack([outer_re, outer_im], axis=-2), (left_re, left_im, right_re, right_im))


def solve(gains, model, corrupted_model, parts, residual, left_hot, right_hot):
    model = model.astype(jnp.float32)
    left_re, left_im, right_re, right_im = parts
    target = residual + corrupted_model
    target_re, target_im = (target[..., 0, :], target[..., 1, :])
    model_re, model_im = (model[..., 0, :], model[..., 1, :])
    weighted_re = target_re * model_re + target_im * model_im
    weighted_im = target_im * model_re - target_re * model_im
    left_num_re = weighted_re * right_re - weighted_im * right_im
    left_num_im = weighted_re * right_im + weighted_im * right_re
    right_num_re = weighted_re * left_re + weighted_im * left_im
    right_num_im = weighted_re * left_im - weighted_im * left_re
    power = model_re * model_re + model_im * model_im
    left_den = power * (right_re * right_re + right_im * right_im)
    right_den = power * (left_re * left_re + left_im * left_im)
    left_products = jnp.sum(jnp.stack([left_num_re, left_num_im, left_den], axis=3), axis=1)
    right_terms = jnp.sum(jnp.stack([right_num_re, right_num_im, right_den], axis=3), axis=1)
    totals = table_dot(left_products, left_hot.T) + table_dot(right_terms, right_hot.T)
    solved = totals[:, :, 0:2] / (totals[:, :, 2:3] + epsilon)
    return (1.0 - step_size) * gains + step_size * solved


def smooth(padded_gains, padded_weights, widths):
    count = widths.shape[0]
    half_width = widths.astype(jnp.float32) * 0.5
    numer = jnp.zeros((padded_gains.shape[0], count) + padded_gains.shape[2:], jnp.float32)
    denom = jnp.zeros((count,), jnp.float32)
    for offset in range(-SPAN, SPAN + 1):
        ratio = offset / half_width
        kernel = jnp.exp(-0.5 * ratio * ratio) * (widths >= abs(offset)).astype(jnp.float32)
        weight_here = kernel * padded_weights[SPAN + offset : SPAN + offset + count]
        numer = (
            numer
            + weight_here[None, :, None, None, None]
            * padded_gains[:, SPAN + offset : SPAN + offset + count]
        )
        denom = denom + weight_here
    return numer / denom[None, :, None, None, None]


def on_device(visibilities, model, gains, weights, widths, baseline_table):
    left_hot, right_hot = station_tables(baseline_table)
    padded_weights = None
    current = gains
    residual = visibilities
    corrupt_all = jax.vmap(corrupt, in_axes=(0, 0, None, None))
    solve_all = jax.vmap(solve, in_axes=(0, 0, 0, 0, None, None, None))
    for sweep in range(ITERS):
        corrupted_model, parts = corrupt_all(current, model, left_hot, right_hot)
        partial_total = jnp.sum(corrupted_model, axis=0)
        total = sum_over_dir(partial_total)
        residual = visibilities - total
        stepped = solve_all(current, model, corrupted_model, parts, residual, left_hot, right_hot)
        if padded_weights is None:
            column = jnp.broadcast_to(weights[None, :, None, None, None], stepped.shape[:-1] + (1,))
            padded = extended(jnp.concatenate([stepped, column], axis=-1), "chan", 1, SPAN)
            padded_gains = padded[..., :-1]
            padded_weights = padded[0, :, 0, 0, -1]
        else:
            padded_gains = extended(stepped, "chan", 1, SPAN)
        current = smooth(padded_gains, padded_weights, widths)
    return (current, residual)


def solution(mesh):
    placed = (
        P("chan", None, None, None, None),
        P("dir", "chan", None, None, None, None),
        P("dir", "chan", None, None, None),
        P("chan"),
        P("chan"),
        P(),
    )
    return jax.shard_map(
        on_device,
        mesh=mesh,
        in_specs=placed,
        out_specs=(P("dir", "chan", None, None, None), P("chan", None, None, None, None)),
        check_vma=False,
    )
```

```python
import jax
import jax.numpy as jnp
from jax import lax
from jax.sharding import PartitionSpec as P

STATIONS = 76
SPAN = 2
ITERS = 2


step_size = 0.6
epsilon = 1e-06
table_precision = lax.Precision.HIGHEST


def extended(cells, axis, dim, width):
    count = lax.axis_size(axis)
    ends = count - 1
    size = cells.shape[dim]
    head = lax.slice_in_dim(cells, 0, width, axis=dim)
    tail = lax.slice_in_dim(cells, size - width, size, axis=dim)
    return jnp.concatenate(
        [
            lax.ppermute(tail, axis, [(i, i + 1) for i in range(ends)]),
            cells,
            lax.ppermute(head, axis, [(i + 1, i) for i in range(ends)]),
        ],
        axis=dim,
    )


def sum_over_dir(partial):
    count = lax.axis_size("dir")
    total = partial
    mask = 1
    while mask < count:
        total = total + lax.ppermute(total, "dir", [(i, i ^ mask) for i in range(count)])
        mask *= 2
    return total


def station_tables(baseline_table):
    column = jnp.arange(STATIONS, dtype=jnp.int32)[:, None]
    left_hot = (baseline_table[0][None, :] == column).astype(jnp.float32)
    right_hot = (baseline_table[1][None, :] == column).astype(jnp.float32)
    return (left_hot, right_hot)


def corrupt(gains, model, left_hot, right_hot):
    model = model.astype(jnp.float32)
    left_gain = jnp.matmul(gains, left_hot, precision=table_precision)[:, None]
    right_gain = jnp.matmul(gains, right_hot, precision=table_precision)[:, None]
    left_re, left_im = (left_gain[..., 0, :], left_gain[..., 1, :])
    right_re, right_im = (right_gain[..., 0, :], right_gain[..., 1, :])
    model_re, model_im = (model[..., 0, :], model[..., 1, :])
    inner_re = left_re * model_re - left_im * model_im
    inner_im = left_re * model_im + left_im * model_re
    outer_re = inner_re * right_re + inner_im * right_im
    outer_im = inner_im * right_re - inner_re * right_im
    return (jnp.stack([outer_re, outer_im], axis=-2), (left_re, left_im, right_re, right_im))


def solve(gains, model, corrupted_model, parts, residual, left_hot, right_hot):
    model = model.astype(jnp.float32)
    left_re, left_im, right_re, right_im = parts
    target = residual + corrupted_model
    target_re, target_im = (target[..., 0, :], target[..., 1, :])
    model_re, model_im = (model[..., 0, :], model[..., 1, :])
    weighted_re = target_re * model_re + target_im * model_im
    weighted_im = target_im * model_re - target_re * model_im
    left_num_re = weighted_re * right_re - weighted_im * right_im
    left_num_im = weighted_re * right_im + weighted_im * right_re
    right_num_re = weighted_re * left_re + weighted_im * left_im
    right_num_im = weighted_re * left_im - weighted_im * left_re
    power = model_re * model_re + model_im * model_im
    left_den = power * (right_re * right_re + right_im * right_im)
    right_den = power * (left_re * left_re + left_im * left_im)
    left_products = jnp.sum(jnp.stack([left_num_re, left_num_im, left_den], axis=3), axis=1)
    right_terms = jnp.sum(jnp.stack([right_num_re, right_num_im, right_den], axis=3), axis=1)
    totals = jnp.matmul(left_products, left_hot.T, precision=table_precision) + jnp.matmul(
        right_terms, right_hot.T, precision=table_precision
    )
    solved = totals[:, :, 0:2] / (totals[:, :, 2:3] + epsilon)
    return (1.0 - step_size) * gains + step_size * solved


def smooth(padded_gains, padded_weights, widths):
    count = widths.shape[0]
    half_width = widths.astype(jnp.float32) * 0.5
    numer = jnp.zeros((padded_gains.shape[0], count) + padded_gains.shape[2:], jnp.float32)
    denom = jnp.zeros((count,), jnp.float32)
    for offset in range(-SPAN, SPAN + 1):
        ratio = offset / half_width
        kernel = jnp.exp(-0.5 * ratio * ratio) * (widths >= abs(offset)).astype(jnp.float32)
        weight_here = kernel * padded_weights[SPAN + offset : SPAN + offset + count]
        numer = (
            numer
            + weight_here[None, :, None, None, None]
            * padded_gains[:, SPAN + offset : SPAN + offset + count]
        )
        denom = denom + weight_here
    return numer / denom[None, :, None, None, None]


def on_device(visibilities, model, gains, weights, widths, baseline_table):
    left_hot, right_hot = station_tables(baseline_table)
    padded_weights = None
    current = gains
    residual = visibilities
    corrupt_all = jax.vmap(corrupt, in_axes=(0, 0, None, None))
    solve_all = jax.vmap(solve, in_axes=(0, 0, 0, 0, None, None, None))
    for sweep in range(ITERS):
        corrupted_model, parts = corrupt_all(current, model, left_hot, right_hot)
        partial_total = jnp.sum(corrupted_model, axis=0)
        total = sum_over_dir(partial_total)
        residual = visibilities - total
        stepped = solve_all(current, model, corrupted_model, parts, residual, left_hot, right_hot)
        residual = -(total - visibilities)
        if padded_weights is None:
            column = jnp.broadcast_to(weights[None, :, None, None, None], stepped.shape[:-1] + (1,))
            padded = extended(jnp.concatenate([stepped, column], axis=-1), "chan", 1, SPAN)
            padded_gains = padded[..., :-1]
            padded_weights = padded[0, :, 0, 0, -1]
        else:
            padded_gains = extended(stepped, "chan", 1, SPAN)
        current = smooth(padded_gains, padded_weights, widths)
    return (current, residual)


def solution(mesh):
    placed = (
        P("chan", None, None, None, None),
        P("dir", "chan", None, None, None, None),
        P("dir", "chan", None, None, None),
        P("chan"),
        P("chan"),
        P(),
    )
    return jax.shard_map(
        on_device,
        mesh=mesh,
        in_specs=placed,
        out_specs=(P("dir", "chan", None, None, None), P("chan", None, None, None, None)),
        check_vma=False,
    )
```

```python
import jax
import jax.numpy as jnp
from jax import lax
from jax.sharding import PartitionSpec as P

STATIONS = 76
SPAN = 2
ITERS = 2


step_size = 0.6
epsilon = 1e-06
table_precision = lax.Precision.HIGHEST


def extended(cells, axis, dim, width):
    count = lax.axis_size(axis)
    ends = count - 1
    size = cells.shape[dim]
    head = lax.slice_in_dim(cells, 0, width, axis=dim)
    tail = lax.slice_in_dim(cells, size - width, size, axis=dim)
    return jnp.concatenate(
        [
            lax.ppermute(tail, axis, [(i, i + 1) for i in range(ends)]),
            cells,
            lax.ppermute(head, axis, [(i + 1, i) for i in range(ends)]),
        ],
        axis=dim,
    )


def sum_over_dir(partial):
    count = lax.axis_size("dir")
    total = partial
    mask = 1
    while mask < count:
        total = total + lax.ppermute(total, "dir", [(i, i ^ mask) for i in range(count)])
        mask *= 2
    return total


def station_tables(baseline_table):
    column = jnp.arange(STATIONS, dtype=jnp.int32)[:, None]
    left_hot = (baseline_table[0][None, :] == column).astype(jnp.float32)
    right_hot = (baseline_table[1][None, :] == column).astype(jnp.float32)
    return (left_hot, right_hot)


def corrupt(gains, model, left_hot, right_hot):
    model = model.astype(jnp.float32)
    left_gain = jnp.matmul(gains, left_hot, precision=table_precision)[:, None]
    right_gain = jnp.matmul(gains, right_hot, precision=table_precision)[:, None]
    left_re, left_im = (left_gain[..., 0, :], left_gain[..., 1, :])
    right_re, right_im = (right_gain[..., 0, :], right_gain[..., 1, :])
    model_re, model_im = (model[..., 0, :], model[..., 1, :])
    inner_re = left_re * model_re - left_im * model_im
    inner_im = left_re * model_im + left_im * model_re
    outer_re = inner_re * right_re + inner_im * right_im
    outer_im = inner_im * right_re - inner_re * right_im
    return (jnp.stack([outer_re, outer_im], axis=-2), (left_re, left_im, right_re, right_im))


def solve(gains, model, corrupted_model, parts, residual, left_hot, right_hot):
    model = model.astype(jnp.float32)
    left_re, left_im, right_re, right_im = parts
    target = residual + corrupted_model
    target_re, target_im = (target[..., 0, :], target[..., 1, :])
    model_re, model_im = (model[..., 0, :], model[..., 1, :])
    weighted_re = target_re * model_re + target_im * model_im
    weighted_im = target_im * model_re - target_re * model_im
    left_num_re = weighted_re * right_re - weighted_im * right_im
    left_num_im = weighted_re * right_im + weighted_im * right_re
    right_num_re = weighted_re * left_re + weighted_im * left_im
    right_num_im = weighted_re * left_im - weighted_im * left_re
    power = model_re * model_re + model_im * model_im
    left_den = power * (right_re * right_re + right_im * right_im)
    right_den = power * (left_re * left_re + left_im * left_im)
    left_products = jnp.sum(jnp.stack([left_num_re, left_num_im], axis=3), axis=1)
    right_terms = jnp.sum(jnp.stack([right_num_re, right_num_im], axis=3), axis=1)
    left_power = jnp.sum(left_den[:, :, :, None], axis=1)
    right_power = jnp.sum(right_den[:, :, :, None], axis=1)
    numer = jnp.matmul(left_products, left_hot.T, precision=table_precision) + jnp.matmul(
        right_terms, right_hot.T, precision=table_precision
    )
    denom = jnp.matmul(left_power, left_hot.T, precision=table_precision) + jnp.matmul(
        right_power, right_hot.T, precision=table_precision
    )
    solved = numer / (denom + epsilon)
    return (1.0 - step_size) * gains + step_size * solved


def smooth(padded_gains, padded_weights, widths):
    count = widths.shape[0]
    half_width = widths.astype(jnp.float32) * 0.5
    numer = jnp.zeros((padded_gains.shape[0], count) + padded_gains.shape[2:], jnp.float32)
    denom = jnp.zeros((count,), jnp.float32)
    for offset in range(-SPAN, SPAN + 1):
        ratio = offset / half_width
        kernel = jnp.exp(-0.5 * ratio * ratio) * (widths >= abs(offset)).astype(jnp.float32)
        weight_here = kernel * padded_weights[SPAN + offset : SPAN + offset + count]
        numer = (
            numer
            + weight_here[None, :, None, None, None]
            * padded_gains[:, SPAN + offset : SPAN + offset + count]
        )
        denom = denom + weight_here
    return numer / denom[None, :, None, None, None]


def on_device(visibilities, model, gains, weights, widths, baseline_table):
    left_hot, right_hot = station_tables(baseline_table)
    padded_weights = None
    current = gains
    residual = visibilities
    corrupt_all = jax.vmap(corrupt, in_axes=(0, 0, None, None))
    solve_all = jax.vmap(solve, in_axes=(0, 0, 0, 0, None, None, None))
    for sweep in range(ITERS):
        corrupted_model, parts = corrupt_all(current, model, left_hot, right_hot)
        partial_total = jnp.sum(corrupted_model, axis=0)
        total = sum_over_dir(partial_total)
        residual = visibilities - total
        stepped = solve_all(current, model, corrupted_model, parts, residual, left_hot, right_hot)
        if padded_weights is None:
            column = jnp.broadcast_to(weights[None, :, None, None, None], stepped.shape[:-1] + (1,))
            padded = extended(jnp.concatenate([stepped, column], axis=-1), "chan", 1, SPAN)
            padded_gains = padded[..., :-1]
            padded_weights = padded[0, :, 0, 0, -1]
        else:
            padded_gains = extended(stepped, "chan", 1, SPAN)
        current = smooth(padded_gains, padded_weights, widths)
    return (current, residual)


def solution(mesh):
    placed = (
        P("chan", None, None, None, None),
        P("dir", "chan", None, None, None, None),
        P("dir", "chan", None, None, None),
        P("chan"),
        P("chan"),
        P(),
    )
    return jax.shard_map(
        on_device,
        mesh=mesh,
        in_specs=placed,
        out_specs=(P("dir", "chan", None, None, None), P("chan", None, None, None, None)),
        check_vma=False,
    )
```
